512 devices in a mesh: tm: 128 (over x, z, core), seg: 4 (over y).
Axes of the slice: x: 4, y: 4, z: 16, core: 2. Of those that a mesh axis runs over, the one named last changes fastest.
Arguments:
- samples: float32 [4, 1048576], P('seg', 'tm'), may hold values from -6 to 6
Outputs:
- cyclic: bfloat16 [4, 256, 8, 64, 2, 256], P('seg', 'tm')
The draws below stay inside these ranges and needn't reach their ends.
All inputs are finite; a program needn't handle non-finite values.
Results may differ from the reference program's by a relative error of at most 0.0084.
Values may be sent and summed in bfloat16 or wider, within the bound.
No kernel may reach another device: no remote copies, remote signals or barrier semaphores. Data moves between devices by JAX's collectives and lax.ppermute only.
A program may use at most 64 MiB of HBM per device.

```python
import math
import jax
import jax.numpy as jnp
from jax import lax

NP = 256
L2 = 256
Q = 8
HOP = 64
FR_SEG = 16384
SEG_LEN = 1048576
N_SEG = 4


def level_of(stream_key, extent, shards, least, largest):
    def one(dim, blocks):
        draws = jax.random.uniform(jax.random.fold_in(jax.random.fold_in(stream_key, 6), dim), (blocks,), jnp.float32, least / len(shards), largest / len(shards))
        return jnp.repeat(jnp.exp(draws), extent[dim] // blocks).reshape((-1,) + (1,) * (len(extent) - dim - 1))

    loudness = one(*shards[0])
    for cut in shards[1:]:
        loudness = loudness * one(*cut)
    return loudness


def scatter_about(stream_key, extent, scale, limit, split=(), kind=jnp.bfloat16):
    entries = scale * jax.random.normal(stream_key, extent, jnp.float32)
    if split:
        entries = entries * level_of(stream_key, extent, split, -0.22, 0.18)
    return jnp.clip(entries, -limit, limit).astype(kind)


def setup_inputs(seed: int = 0) -> dict:
    key_list = jax.random.split(jax.random.key(seed), 2)
    samples = scatter_about(key_list[0], (N_SEG, SEG_LEN), 1.0, 6.0, ((0, 4), (1, 128)), jnp.float32)
    return dict(samples=samples)


def channelize(stream, frame_count, channels):
    hop_len = channels // 4
    rows = stream.reshape(frame_count + 3, hop_len).T
    frames = jnp.concatenate([rows[:, offset:offset + frame_count] for offset in range(4)], axis=0)
    sample_pos = jnp.arange(channels, dtype=jnp.int32)
    window = (0.5 - 0.5 * jnp.cos(2.0 * math.pi * sample_pos.astype(jnp.float32) / channels)) / math.sqrt(3.0 * channels / 8.0)
    windowed = (frames * window[:, None]).astype(jnp.bfloat16)
    product_idx = sample_pos[:, None] * sample_pos[None, :] % channels
    angles = 2.0 * math.pi * product_idx.astype(jnp.float32) / channels
    dft_table = jnp.concatenate([jnp.cos(angles), -jnp.sin(angles)], axis=0).astype(jnp.bfloat16)
    raw = jnp.dot(dft_table, windowed, preferred_element_type=jnp.float32)
    real_raw = raw[:channels]
    imag_raw = raw[channels:]
    frame_pos = jnp.arange(frame_count, dtype=jnp.int32)
    quarter = sample_pos[:, None] * frame_pos[None, :] % 4
    real_out = jnp.where(quarter == 0, real_raw, jnp.where(quarter == 1, imag_raw, jnp.where(quarter == 2, -real_raw, -imag_raw)))
    imag_out = jnp.where(quarter == 0, imag_raw, jnp.where(quarter == 1, -real_raw, jnp.where(quarter == 2, -imag_raw, real_raw)))
    return jnp.stack([real_out, imag_out]).astype(jnp.bfloat16)

def second_table(length):
    positions = jnp.arange(length, dtype=jnp.int32)
    angles = 2.0 * math.pi * (positions[:, None] * positions[None, :] % length).astype(jnp.float32) / length
    cosine = jnp.cos(angles) / math.sqrt(length)
    sine = jnp.sin(angles) / math.sqrt(length)
    upper = jnp.stack([cosine, -sine], axis=1)
    lower = jnp.stack([sine, cosine], axis=1)
    return jnp.stack([upper, lower]).astype(jnp.bfloat16)

def pair_products(own_block, partner_block):
    own_real = own_block[0].astype(jnp.float32)
    own_imag = own_block[1].astype(jnp.float32)
    other_real = partner_block[0].astype(jnp.float32)
    other_imag = partner_block[1].astype(jnp.float32)
    return jnp.stack([own_real * other_real + own_imag * other_imag, own_imag * other_real - own_real * other_imag]).astype(jnp.bfloat16)

def transform(products, dft_table, length):
    shaped = products.reshape(2, products.shape[1], products.shape[2] // length, length)
    result = jnp.einsum('ckbj,cjof->kbof', shaped.astype(jnp.float32), dft_table.astype(jnp.float32))
    return result.astype(jnp.bfloat16)

def reference(samples):
    stream = jnp.concatenate([samples.reshape(-1), jnp.zeros((3 * HOP,), jnp.float32)])
    dft_table = second_table(L2)

    def one_segment(seg_idx):
        piece = lax.dynamic_slice_in_dim(stream, seg_idx * SEG_LEN, SEG_LEN + 3 * HOP)
        spectra = channelize(piece, FR_SEG, NP)
        extended = jnp.concatenate([spectra, spectra[:, :Q - 1]], axis=1)

        def one_offset(offset):
            partner = lax.dynamic_slice_in_dim(extended, offset, NP, 1)
            return transform(pair_products(spectra, partner), dft_table, L2)
        result = lax.map(one_offset, jnp.arange(Q, dtype=jnp.int32))
        return jnp.transpose(result, (1, 0, 2, 3, 4))
    return lax.map(one_segment, jnp.arange(N_SEG, dtype=jnp.int32))
```

```python
import math

import jax
import jax.numpy as jnp
from jax import lax
from jax.sharding import PartitionSpec as P

NP = 256
L2 = 256
Q = 8


def passed_along(value, axis, by):
    length = lax.axis_size(axis)
    return lax.ppermute(value, axis, [(i, (i + by) % length) for i in range(length)])


def channelize(stream, frame_count, channels):
    hop_len = channels // 4
    rows = stream.reshape(frame_count + 3, hop_len).T
    frames = jnp.concatenate(
        [rows[:, offset : offset + frame_count] for offset in range(4)], axis=0
    )
    sample_pos = jnp.arange(channels, dtype=jnp.int32)
    window = (
        0.5 - 0.5 * jnp.cos(2.0 * math.pi * sample_pos.astype(jnp.float32) / channels)
    ) / math.sqrt(3.0 * channels / 8.0)
    windowed = (frames * window[:, None]).astype(jnp.bfloat16)
    product_idx = sample_pos[:, None] * sample_pos[None, :] % channels
    angles = 2.0 * math.pi * product_idx.astype(jnp.float32) / channels
    dft_table = jnp.concatenate([jnp.cos(angles), -jnp.sin(angles)], axis=0).astype(jnp.bfloat16)
    raw = jnp.dot(dft_table, windowed, preferred_element_type=jnp.float32)
    real_raw = raw[:channels]
    imag_raw = raw[channels:]
    frame_pos = jnp.arange(frame_count, dtype=jnp.int32)
    quarter = sample_pos[:, None] * frame_pos[None, :] % 4
    real_out = jnp.where(
        quarter == 0,
        real_raw,
        jnp.where(quarter == 1, imag_raw, jnp.where(quarter == 2, -real_raw, -imag_raw)),
    )
    imag_out = jnp.where(
        quarter == 0,
        imag_raw,
        jnp.where(quarter == 1, -real_raw, jnp.where(quarter == 2, -imag_raw, real_raw)),
    )
    return jnp.stack([real_out, imag_out]).astype(jnp.bfloat16)


def second_table(length):
    positions = jnp.arange(length, dtype=jnp.int32)
    angles = (
        2.0
        * math.pi
        * (positions[:, None] * positions[None, :] % length).astype(jnp.float32)
        / length
    )
    cosine = jnp.cos(angles) / math.sqrt(length)
    sine = jnp.sin(angles) / math.sqrt(length)
    upper = jnp.stack([cosine, -sine], axis=1)
    lower = jnp.stack([sine, cosine], axis=1)
    return jnp.stack([upper, lower]).astype(jnp.bfloat16)


def pair_products(own_block, partner_block):
    own_real = own_block[0].astype(jnp.float32)
    own_imag = own_block[1].astype(jnp.float32)
    other_real = partner_block[0].astype(jnp.float32)
    other_imag = partner_block[1].astype(jnp.float32)
    return jnp.stack(
        [
            own_real * other_real + own_imag * other_imag,
            own_imag * other_real - own_real * other_imag,
        ]
    ).astype(jnp.bfloat16)


def transform(products, dft_table, length):
    shaped = products.reshape(2, products.shape[1], products.shape[2] // length, length)
    return jnp.einsum("ckbj,cjof->kbof", shaped, dft_table, preferred_element_type=jnp.float32)


def body(samples):
    tm_count = lax.axis_size("tm")
    seg_count = lax.axis_size("seg")
    hop_len = NP // 4
    frame_count = samples.shape[1] // hop_len
    head_rim = samples[:, : 3 * hop_len]
    def flat(s, t):
        return t * seg_count + s

    pairs = [(flat(s, t), flat(s, t - 1)) for s in range(seg_count) for t in range(1, tm_count)]
    pairs += [(flat(s + 1, 0), flat(s, tm_count - 1)) for s in range(seg_count - 1)]
    tail_rim = lax.ppermute(head_rim, ("tm", "seg"), pairs)
    stream = jnp.concatenate([samples, tail_rim], axis=1).reshape(-1)
    spectra = channelize(stream, frame_count, NP)
    per_dev = NP // tm_count
    gathered = lax.all_to_all(spectra, "tm", split_axis=1, concat_axis=2, tiled=True)
    pieces = [gathered]
    need = Q - 1
    offset = 1
    while need > 0:
        take = min(per_dev, need)
        pieces.append(passed_along(gathered[:, :take], "tm", -offset))
        need -= take
        offset += 1
    extended = jnp.concatenate(pieces, axis=1)
    own_block = extended[:, :per_dev]
    dft_table = second_table(L2)
    results = []
    for offset in range(Q):
        partner = extended[:, offset : offset + per_dev]
        results.append(
            transform(pair_products(own_block, partner), dft_table, L2).astype(jnp.bfloat16)
        )
    return jnp.stack(results, axis=1)[None]


def solution(mesh):
    return jax.shard_map(
        body,
        mesh=mesh,
        in_specs=(P("seg", "tm"),),
        out_specs=P("seg", "tm", None, None, None, None),
        check_vma=False,
    )
```

```python
import math

import jax
import numpy as np
import jax.numpy as jnp
from jax import lax
from jax.sharding import PartitionSpec as P

NP = 256
L2 = 256
Q = 8


def passed_along(value, axis, by):
    length = lax.axis_size(axis)
    return lax.ppermute(value, axis, [(i, (i + by) % length) for i in range(length)])


def channelize(stream, frame_count, channels):
    hop_len = channels // 4
    rows = stream.reshape(frame_count + 3, hop_len).T
    frames = jnp.concatenate(
        [rows[:, offset : offset + frame_count] for offset in range(4)], axis=0
    )
    sample_pos = jnp.arange(channels, dtype=jnp.int32)
    window = (
        0.5 - 0.5 * jnp.cos(2.0 * math.pi * sample_pos.astype(jnp.float32) / channels)
    ) / math.sqrt(3.0 * channels / 8.0)
    windowed = (frames * window[:, None]).astype(jnp.bfloat16)
    dft_table = jnp.asarray(first_table(channels))
    raw = jnp.dot(dft_table, windowed, preferred_element_type=jnp.float32)
    real_raw = raw[:channels]
    imag_raw = raw[channels:]
    frame_pos = jnp.arange(frame_count, dtype=jnp.int32)
    quarter = sample_pos[:, None] * frame_pos[None, :] % 4
    real_out = jnp.where(
        quarter == 0,
        real_raw,
        jnp.where(quarter == 1, imag_raw, jnp.where(quarter == 2, -real_raw, -imag_raw)),
    )
    imag_out = jnp.where(
        quarter == 0,
        imag_raw,
        jnp.where(quarter == 1, -real_raw, jnp.where(quarter == 2, -imag_raw, real_raw)),
    )
    return jnp.stack([real_out, imag_out]).astype(jnp.bfloat16)


def table_angles(length):
    positions = np.arange(length, dtype=np.int64)
    product_idx = (positions[:, None] * positions[None, :] % length).astype(np.float32)
    return (np.float32(2.0 * math.pi) * product_idx / np.float32(length)).astype(np.float64)


def first_table(channels):
    angles = table_angles(channels)
    cosine = np.cos(angles).astype(np.float32)
    sine = np.sin(angles).astype(np.float32)
    return np.concatenate([cosine, -sine], axis=0).astype(jnp.bfloat16)


def second_table(length):
    angles = table_angles(length)
    cosine = np.cos(angles).astype(np.float32) / np.float32(math.sqrt(length))
    sine = np.sin(angles).astype(np.float32) / np.float32(math.sqrt(length))
    upper = np.stack([cosine, -sine], axis=1)
    lower = np.stack([sine, cosine], axis=1)
    return jnp.asarray(np.stack([upper, lower]).astype(jnp.bfloat16))


def pair_products(own_block, partner_block):
    own_real = own_block[0].astype(jnp.float32)
    own_imag = own_block[1].astype(jnp.float32)
    other_real = partner_block[0].astype(jnp.float32)
    other_imag = partner_block[1].astype(jnp.float32)
    return jnp.stack(
        [
            own_real * other_real + own_imag * other_imag,
            own_imag * other_real - own_real * other_imag,
        ]
    ).astype(jnp.bfloat16)


def transform(products, dft_table, length):
    shaped = products.reshape(2, products.shape[1], products.shape[2] // length, length)
    return jnp.einsum("ckbj,cjof->kbof", shaped, dft_table, preferred_element_type=jnp.float32)


def body(samples):
    tm_count = lax.axis_size("tm")
    seg_count = lax.axis_size("seg")
    hop_len = NP // 4
    frame_count = samples.shape[1] // hop_len
    head_rim = samples[:, : 3 * hop_len]
    def flat(s, t):
        return t * seg_count + s

    pairs = [(flat(s, t), flat(s, t - 1)) for s in range(seg_count) for t in range(1, tm_count)]
    pairs += [(flat(s + 1, 0), flat(s, tm_count - 1)) for s in range(seg_count - 1)]
    tail_rim = lax.ppermute(head_rim, ("tm", "seg"), pairs)
    stream = jnp.concatenate([samples, tail_rim], axis=1).reshape(-1)
    spectra = channelize(stream, frame_count, NP)
    per_dev = NP // tm_count
    gathered = lax.all_to_all(spectra, "tm", split_axis=1, concat_axis=2, tiled=True)
    pieces = [gathered]
    need = Q - 1
    offset = 1
    while need > 0:
        take = min(per_dev, need)
        pieces.append(passed_along(gathered[:, :take], "tm", -offset))
        need -= take
        offset += 1
    extended = jnp.concatenate(pieces, axis=1)
    own_block = extended[:, :per_dev]
    dft_table = second_table(L2)
    results = []
    for offset in range(Q):
        partner = extended[:, offset : offset + per_dev]
        results.append(
            transform(pair_products(own_block, partner), dft_table, L2).astype(jnp.bfloat16)
        )
    return jnp.stack(results, axis=1)[None]


def solution(mesh):
    return jax.shard_map(
        body,
        mesh=mesh,
        in_specs=(P("seg", "tm"),),
        out_specs=P("seg", "tm", None, None, None, None),
        check_vma=False,
    )
```

```python
import math

import jax
import numpy as np
import jax.numpy as jnp
from jax import lax
from jax.sharding import PartitionSpec as P

NP = 256
L2 = 256
Q = 8


def passed_along(value, axis, by):
    length = lax.axis_size(axis)
    return lax.ppermute(value, axis, [(i, (i + by) % length) for i in range(length)])


def channelize(stream, frame_count, channels, dft_table):
    hop_len = channels // 4
    rows = stream.reshape(frame_count + 3, hop_len).T
    frames = jnp.concatenate(
        [rows[:, offset : offset + frame_count] for offset in range(4)], axis=0
    )
    sample_pos = jnp.arange(channels, dtype=jnp.int32)
    window = (
        0.5 - 0.5 * jnp.cos(2.0 * math.pi * sample_pos.astype(jnp.float32) / channels)
    ) / math.sqrt(3.0 * channels / 8.0)
    windowed = (frames * window[:, None]).astype(jnp.bfloat16)
    raw = jnp.dot(dft_table, windowed, preferred_element_type=jnp.float32)
    real_raw = raw[:channels]
    imag_raw = raw[channels:]
    frame_pos = jnp.arange(frame_count, dtype=jnp.int32)
    quarter = sample_pos[:, None] * frame_pos[None, :] % 4
    real_out = jnp.where(
        quarter == 0,
        real_raw,
        jnp.where(quarter == 1, imag_raw, jnp.where(quarter == 2, -real_raw, -imag_raw)),
    )
    imag_out = jnp.where(
        quarter == 0,
        imag_raw,
        jnp.where(quarter == 1, -real_raw, jnp.where(quarter == 2, -imag_raw, real_raw)),
    )
    return jnp.stack([real_out, imag_out]).astype(jnp.bfloat16)


def table_angles(length):
    positions = np.arange(length, dtype=np.int64)
    product_idx = (positions[:, None] * positions[None, :] % length).astype(np.float32)
    return (np.float32(2.0 * math.pi) * product_idx / np.float32(length)).astype(np.float64)


def first_table(channels):
    angles = table_angles(channels)
    cosine = np.cos(angles).astype(np.float32)
    sine = np.sin(angles).astype(np.float32)
    return np.concatenate([cosine, -sine], axis=0).astype(jnp.bfloat16)


def second_table(length):
    angles = table_angles(length)
    cosine = np.cos(angles).astype(np.float32) / np.float32(math.sqrt(length))
    sine = np.sin(angles).astype(np.float32) / np.float32(math.sqrt(length))
    upper = np.stack([cosine, -sine], axis=1)
    lower = np.stack([sine, cosine], axis=1)
    return jnp.asarray(np.stack([upper, lower]).astype(jnp.bfloat16))


def pair_products(own_block, partner_block):
    own_real = own_block[0].astype(jnp.float32)
    own_imag = own_block[1].astype(jnp.float32)
    other_real = partner_block[0].astype(jnp.float32)
    other_imag = partner_block[1].astype(jnp.float32)
    return jnp.stack(
        [
            own_real * other_real + own_imag * other_imag,
            own_imag * other_real - own_real * other_imag,
        ]
    ).astype(jnp.bfloat16)


def transform(products, dft_table, length):
    shaped = products.reshape(2, products.shape[1], products.shape[2] // length, length)
    return jnp.einsum("ckbj,cjof->kbof", shaped, dft_table, preferred_element_type=jnp.float32)


def body(samples):
    tm_count = lax.axis_size("tm")
    seg_count = lax.axis_size("seg")
    hop_len = NP // 4
    frame_count = samples.shape[1] // hop_len
    head_rim = samples[:, : 3 * hop_len]
    unit = (samples[0, 0] * 0.0 + 1.0).astype(jnp.bfloat16)
    dft_table = lax.optimization_barrier(jnp.asarray(first_table(NP)) * unit)
    def flat(s, t):
        return t * seg_count + s

    pairs = [(flat(s, t), flat(s, t - 1)) for s in range(seg_count) for t in range(1, tm_count)]
    pairs += [(flat(s + 1, 0), flat(s, tm_count - 1)) for s in range(seg_count - 1)]
    tail_rim = lax.ppermute(head_rim, ("tm", "seg"), pairs)
    stream = jnp.concatenate([samples, tail_rim], axis=1).reshape(-1)
    spectra = channelize(stream, frame_count, NP, dft_table)
    per_dev = NP // tm_count
    gathered = lax.all_to_all(spectra, "tm", split_axis=1, concat_axis=2, tiled=True)
    pieces = [gathered]
    need = Q - 1
    offset = 1
    while need > 0:
        take = min(per_dev, need)
        pieces.append(passed_along(gathered[:, :take], "tm", -offset))
        need -= take
        offset += 1
    extended = jnp.concatenate(pieces, axis=1)
    own_block = extended[:, :per_dev]
    dft_table = second_table(L2)
    results = []
    for offset in range(Q):
        partner = extended[:, offset : offset + per_dev]
        results.append(
            transform(pair_products(own_block, partner), dft_table, L2).astype(jnp.bfloat16)
        )
    return jnp.stack(results, axis=1)[None]


def solution(mesh):
    return jax.shard_map(
        body,
        mesh=mesh,
        in_specs=(P("seg", "tm"),),
        out_specs=P("seg", "tm", None, None, None, None),
        check_vma=False,
    )
```

```python
import math

import jax
import numpy as np
import jax.numpy as jnp
from jax import lax
from jax.sharding import PartitionSpec as P

NP = 256
L2 = 256
Q = 8


def passed_along(value, axis, by):
    length = lax.axis_size(axis)
    return lax.ppermute(value, axis, [(i, (i + by) % length) for i in range(length)])


def channelize(stream, frame_count, channels, dft_table):
    hop_len = channels // 4
    rows = stream.reshape(frame_count + 3, hop_len).T
    frames = jnp.concatenate(
        [rows[:, offset : offset + frame_count] for offset in range(4)], axis=0
    )
    sample_pos = jnp.arange(channels, dtype=jnp.int32)
    window = (
        0.5 - 0.5 * jnp.cos(2.0 * math.pi * sample_pos.astype(jnp.float32) / channels)
    ) / math.sqrt(3.0 * channels / 8.0)
    windowed = (frames * window[:, None]).astype(jnp.bfloat16)
    raw = jnp.dot(dft_table, windowed, preferred_element_type=jnp.float32)
    real_raw = raw[:channels]
    imag_raw = raw[channels:]
    frame_pos = jnp.arange(frame_count, dtype=jnp.int32)
    quarter = sample_pos[:, None] * frame_pos[None, :] % 4
    real_out = jnp.where(
        quarter == 0,
        real_raw,
        jnp.where(quarter == 1, imag_raw, jnp.where(quarter == 2, -real_raw, -imag_raw)),
    )
    imag_out = jnp.where(
        quarter == 0,
        imag_raw,
        jnp.where(quarter == 1, -real_raw, jnp.where(quarter == 2, -imag_raw, real_raw)),
    )
    return jnp.stack([real_out, imag_out]).astype(jnp.bfloat16)


def table_angles(length):
    positions = np.arange(length, dtype=np.int64)
    product_idx = (positions[:, None] * positions[None, :] % length).astype(np.float32)
    return (np.float32(2.0 * math.pi) * product_idx / np.float32(length)).astype(np.float64)


def first_table(channels):
    angles = table_angles(channels)
    cosine = np.cos(angles).astype(np.float32)
    sine = np.sin(angles).astype(np.float32)
    return np.concatenate([cosine, -sine], axis=0).astype(jnp.bfloat16)


def second_table(length):
    angles = table_angles(length)
    cosine = np.cos(angles).astype(np.float32) / np.float32(math.sqrt(length))
    sine = np.sin(angles).astype(np.float32) / np.float32(math.sqrt(length))
    upper = np.stack([cosine, -sine], axis=1)
    lower = np.stack([sine, cosine], axis=1)
    return jnp.asarray(np.stack([upper, lower]).astype(jnp.bfloat16))


def pair_products(own_block, partner_block):
    own_real = own_block[0].astype(jnp.float32)
    own_imag = own_block[1].astype(jnp.float32)
    other_real = partner_block[0].astype(jnp.float32)
    other_imag = partner_block[1].astype(jnp.float32)
    return jnp.stack(
        [
            own_real * other_real + own_imag * other_imag,
            own_imag * other_real - own_real * other_imag,
        ]
    ).astype(jnp.bfloat16)


def transform(products, dft_table, length):
    shaped = products.reshape(2, products.shape[1], products.shape[2] // length, length)
    return jnp.einsum("ckbj,cjof->kbof", shaped, dft_table, preferred_element_type=jnp.float32)


def body(samples):
    tm_count = lax.axis_size("tm")
    seg_count = lax.axis_size("seg")
    hop_len = NP // 4
    frame_count = samples.shape[1] // hop_len
    head_rim = samples[:, : 3 * hop_len]
    unit = (lax.axis_index("tm") >= 0).astype(jnp.bfloat16)
    dft_table = lax.optimization_barrier(jnp.asarray(first_table(NP)) * unit)
    def flat(s, t):
        return t * seg_count + s

    pairs = [(flat(s, t), flat(s, t - 1)) for s in range(seg_count) for t in range(1, tm_count)]
    pairs += [(flat(s + 1, 0), flat(s, tm_count - 1)) for s in range(seg_count - 1)]
    tail_rim = lax.ppermute(head_rim, ("tm", "seg"), pairs)
    stream = jnp.concatenate([samples, tail_rim], axis=1).reshape(-1)
    spectra = channelize(stream, frame_count, NP, dft_table)
    per_dev = NP // tm_count
    gathered = lax.all_to_all(spectra, "tm", split_axis=1, concat_axis=2, tiled=True)
    pieces = [gathered]
    need = Q - 1
    offset = 1
    while need > 0:
        take = min(per_dev, need)
        pieces.append(passed_along(gathered[:, :take], "tm", -offset))
        need -= take
        offset += 1
    extended = jnp.concatenate(pieces, axis=1)
    own_block = extended[:, :per_dev]
    dft_table = second_table(L2)
    results = []
    for offset in range(Q):
        partner = extended[:, offset : offset + per_dev]
        results.append(
            transform(pair_products(own_block, partner), dft_table, L2).astype(jnp.bfloat16)
        )
    return jnp.stack(results, axis=1)[None]


def solution(mesh):
    return jax.shard_map(
        body,
        mesh=mesh,
        in_specs=(P("seg", "tm"),),
        out_specs=P("seg", "tm", None, None, None, None),
        check_vma=False,
    )
```
